512 devices in a mesh: aux: 16 (over x, y_lo, core), row: 32 (over y_hi, z).
Axes of the slice: x: 4, y: 4 (y_hi: 2, y_lo: 2; y = y_hi * 2 + y_lo), z: 16, core: 2. Of those that a mesh axis runs over, the one named last changes fastest.
Arguments:
- chol_vectors: bfloat16 [16, 6144, 6144], P('aux', 'row'), may hold values from -0.078125 to 0.078125
- occ_coeff: bfloat16 [6144, 512], P('row'), may hold values from -4 to 4
- tile_pairs: int32 [528, 2], replicated, may hold values from 0 to 31, as said below
- tile_owner: int32 [32, 17], P('row'), may hold values from 0 to 527, as said below
Outputs:
- ktiles: float32 [544, 192, 192], P('row', 'aux')
The draws below stay inside these ranges and needn't reach their ends.
Inputs may be any that keep to these rules, and one draw needn't show every extreme that they name: `tile_pairs`: each entry is a pair (i, j) with i <= j, and every such pair of 32 blocks appears exactly once. `tile_owner`: every tile index appears at least once, a few twice.
All inputs are finite; a program needn't handle non-finite values.
Results may differ from the reference program's by a relative error of at most 0.0022.
Values may be sent and summed in bfloat16 or wider, within the bound.
No kernel may reach another device: no remote copies, remote signals or barrier semaphores. Data moves between devices by JAX's collectives and lax.ppermute only.
A program may use at most 64 MiB of HBM per device.

```python
import jax
import jax.numpy as jnp
import numpy as np
from jax import lax

NBF = 6144
NOCC = 512
NQ = 16
NBLK = 32
BLK = 192
N_TILES = 528
SLOTS = 17


def draw_tile_pairs(key, part):
    upper_rows, upper_cols = np.triu_indices(NBLK)
    listed = jnp.stack([jnp.asarray(upper_rows, jnp.int32), jnp.asarray(upper_cols, jnp.int32)], axis=1)
    order = jax.random.permutation(key, N_TILES)
    return listed[order].astype(jnp.int32)


def draw_tile_owner(key, part):
    order = jax.random.permutation(jax.random.fold_in(key, 7), NBLK * SLOTS)
    return (order % N_TILES).astype(jnp.int32).reshape(NBLK, SLOTS)


def levels(own_key, shape, cuts, smallest, high):
    loudness = 1.0
    for position, shards_of in cuts:
        steps = jax.random.uniform(jax.random.fold_in(jax.random.fold_in(own_key, 6), position), (shards_of,), jnp.float32, smallest / len(cuts), high / len(cuts))
        loudness = loudness * jnp.repeat(jnp.exp(steps), shape[position] // shards_of).reshape((-1,) + (1,) * (len(shape) - 1 - position))
    return loudness


def scatter_about(stream_key, shape, width, limit, shards=(), kind=jnp.bfloat16):
    entries = jax.random.normal(stream_key, shape, jnp.float32) * width
    if len(shards) > 0:
        entries = levels(stream_key, shape, shards, -0.22, 0.18) * entries
    return jnp.clip(entries, min=-limit, max=limit).astype(kind)


def setup_inputs(seed: int = 0) -> dict:
    streams_of = jax.random.split(jax.random.key(seed), 5)
    chol_vectors = scatter_about(streams_of[0], (NQ, NBF, NBF), NBF ** -0.5, 0.078125, ((0, 16), (1, 32)))
    occ_coeff = scatter_about(streams_of[1], (NBF, NOCC), 0.5, 4.0, ((0, 32),))
    tile_pairs = draw_tile_pairs(jax.random.fold_in(streams_of[4], 71), 0)
    tile_owner = draw_tile_owner(jax.random.fold_in(streams_of[4], 71), 0)
    return {"chol_vectors": chol_vectors, "occ_coeff": occ_coeff, "tile_pairs": tile_pairs, "tile_owner": tile_owner}


def reference(chol_vectors, occ_coeff, tile_pairs, tile_owner):
    def transform(matrix):
        return jnp.dot(matrix, occ_coeff, preferred_element_type=jnp.float32).astype(jnp.bfloat16)

    half = lax.map(transform, chol_vectors)
    nvec = half.shape[0]
    blocks = half.reshape(nvec, NBLK, BLK, NOCC)
    flat_owner = tile_owner.reshape(-1)

    def one_tile(index):
        left = jnp.take(blocks, tile_pairs[index, 0], axis=1).astype(jnp.float32)
        right = jnp.take(blocks, tile_pairs[index, 1], axis=1).astype(jnp.float32)
        return jnp.einsum("qao,qbo->ab", left, right)

    return lax.map(one_tile, flat_owner)
```

```python
import jax
import jax.numpy as jnp
from jax import lax
from jax.sharding import PartitionSpec as P


def local(chol_vectors, occ_coeff, tile_pairs, tile_owner):
    block = chol_vectors.shape[1]
    nocc = occ_coeff.shape[1]
    nblk = lax.axis_size("row")
    naux = lax.axis_size("aux")
    half_cols = nocc // 2

    core = lax.axis_index("aux") % 2
    mine = lax.dynamic_slice_in_dim(occ_coeff, core * half_cols, half_cols, 1)
    mine_full = lax.all_gather(mine, "row", axis=0, tiled=True)
    partner = [(i, i ^ 1) for i in range(naux)]
    other_full = lax.ppermute(mine_full, "aux", partner)

    chol = chol_vectors[0]
    half_mine = jnp.dot(chol, mine_full, preferred_element_type=jnp.float32).astype(jnp.bfloat16)
    half_other = jnp.dot(chol, other_full, preferred_element_type=jnp.float32).astype(jnp.bfloat16)
    half = jnp.where(
        core == 0,
        jnp.concatenate([half_mine, half_other], axis=1),
        jnp.concatenate([half_other, half_mine], axis=1),
    )

    gathered = lax.all_gather(half, "row", axis=0, tiled=True)
    blocks = gathered.reshape(nblk, block, nocc)
    chosen = tile_pairs[tile_owner[0]]
    left_rows = jnp.take(blocks, chosen[:, 0], axis=0)
    right_rows = jnp.take(blocks, chosen[:, 1], axis=0)
    partial_tiles = jnp.einsum(
        "sao,sbo->sab", left_rows, right_rows, preferred_element_type=jnp.float32
    )
    slots = partial_tiles.shape[0]
    split = partial_tiles.reshape(slots, naux, block // naux, block).transpose(1, 0, 2, 3)
    pieces = lax.all_to_all(split, "aux", 0, 0, tiled=True)
    return jnp.sum(pieces, axis=0)


def solution(mesh):
    placed = (P("aux", "row", None), P("row", None), P(), P("row", None))
    return jax.shard_map(
        local, mesh=mesh, in_specs=placed, out_specs=P("row", "aux", None), check_vma=False
    )
```

```python
import jax
import jax.numpy as jnp
from jax import lax
from jax.sharding import PartitionSpec as P


def ring_gather(x, nrow, ring):
    pairs = nrow // ring
    r = lax.axis_index("row")
    yh = r // ring
    z = r % ring
    other = lax.ppermute(x, "row", [(i, i ^ ring) for i in range(nrow)])
    pair = jnp.where(yh == 0, jnp.stack([x, other]), jnp.stack([other, x]))
    send_right = [(i, (i // ring) * ring + (i % ring + 1) % ring) for i in range(nrow)]
    send_left = [(i, (i // ring) * ring + (i % ring - 1) % ring) for i in range(nrow)]
    got = [None] * ring
    got[0] = pair
    from_left = pair
    from_right = pair
    for t in range(1, ring // 2):
        from_left = lax.ppermute(from_left, "row", send_right)
        from_right = lax.ppermute(from_right, "row", send_left)
        got[t] = from_left
        got[ring - t] = from_right
    low = lax.ppermute(from_left[0], "row", send_right)
    high = lax.ppermute(from_right[1], "row", send_left)
    got[ring // 2] = jnp.stack([low, high])
    stacked = jnp.stack(got)
    return stacked.reshape((ring * pairs,) + x.shape), z


def position_of(k, z, ring):
    return ((z - k % ring) % ring) * 2 + k // ring


def local(chol_vectors, occ_coeff, tile_pairs, tile_owner):
    block = chol_vectors.shape[1]
    nbf = chol_vectors.shape[2]
    nocc = occ_coeff.shape[1]
    nrow = lax.axis_size("row")
    naux = lax.axis_size("aux")
    ring = nrow // 2
    half_cols = nocc // 2

    core = lax.axis_index("aux") % 2
    mine = lax.dynamic_slice_in_dim(occ_coeff, core * half_cols, half_cols, 1)
    mine_ring, z = ring_gather(mine, nrow, ring)
    partner = [(i, i ^ 1) for i in range(naux)]
    other_ring = lax.ppermute(mine_ring, "aux", partner)
    coeff_ring = jnp.where(
        core == 0,
        jnp.concatenate([mine_ring, other_ring], axis=2),
        jnp.concatenate([other_ring, mine_ring], axis=2),
    )

    p = jnp.arange(nrow)
    block_at = (p % 2) * ring + (z - p // 2) % ring
    chol = chol_vectors[0].reshape(block, nrow, nbf // nrow)
    chol_ring = jnp.take(chol, block_at, axis=1).reshape(block, nbf)
    half = jnp.dot(
        chol_ring, coeff_ring.reshape(nbf, nocc), preferred_element_type=jnp.float32
    ).astype(jnp.bfloat16)

    half_ring, _ = ring_gather(half, nrow, ring)
    chosen = tile_pairs[tile_owner[0]]
    left_rows = jnp.take(half_ring, position_of(chosen[:, 0], z, ring), axis=0)
    right_rows = jnp.take(half_ring, position_of(chosen[:, 1], z, ring), axis=0)
    partial_tiles = jnp.einsum(
        "sao,sbo->sab", left_rows, right_rows, preferred_element_type=jnp.float32
    )
    slots = partial_tiles.shape[0]
    split = partial_tiles.reshape(slots, naux, block // naux, block).transpose(1, 0, 2, 3)
    pieces = lax.all_to_all(split, "aux", 0, 0, tiled=True)
    return jnp.sum(pieces, axis=0)


def solution(mesh):
    placed = (P("aux", "row", None), P("row", None), P(), P("row", None))
    return jax.shard_map(
        local, mesh=mesh, in_specs=placed, out_specs=P("row", "aux", None), check_vma=False
    )
```

```python
import jax
import jax.numpy as jnp
from jax import lax
from jax.sharding import PartitionSpec as P


def y_pair(x, nrow, ring):
    yh = lax.axis_index("row") // ring
    other = lax.ppermute(x, "row", [(i, i ^ ring) for i in range(nrow)])
    return jnp.where(yh == 0, jnp.stack([x, other]), jnp.stack([other, x]))


def one_way_ring(x, naux, nrow, ring):
    perm = []
    for a in range(naux):
        for r in range(nrow):
            base = (r // ring) * ring
            step = 1 if a % 2 == 0 else -1
            perm.append((a * nrow + r, a * nrow + base + (r % ring + step) % ring))
    got = []
    for _ in range(ring // 2):
        x = lax.ppermute(x, ("aux", "row"), perm)
        got.append(x)
    return jnp.stack(got)


def slot_of(k, z, core, ring):
    y = k // ring
    d = (z - k % ring) % ring
    hr = ring // 2
    idx0 = jnp.where(d == 0, 0, jnp.where(d <= hr, d, hr + ring - d))
    idx1 = jnp.where(d == 0, 0, jnp.where(d >= hr, ring - d, hr + d))
    return jnp.where(core == 0, idx0, idx1) * 2 + y


def local(chol_vectors, occ_coeff, tile_pairs, tile_owner):
    block = chol_vectors.shape[1]
    nbf = chol_vectors.shape[2]
    nocc = occ_coeff.shape[1]
    nrow = lax.axis_size("row")
    naux = lax.axis_size("aux")
    ring = nrow // 2
    core = lax.axis_index("aux") % 2
    z = lax.axis_index("row") % ring
    partner = [(i, i ^ 1) for i in range(naux)]
    k = jnp.arange(nrow)

    pair_c = y_pair(occ_coeff, nrow, ring)
    stream_c = one_way_ring(pair_c, naux, nrow, ring)
    swapped_c = lax.ppermute(stream_c, "aux", partner)
    all_c = jnp.concatenate([pair_c[None], stream_c, swapped_c]).reshape(
        (-1, block, nocc)
    )
    coeff = jnp.take(all_c, slot_of(k, z, core, ring), axis=0).reshape(nbf, nocc)
    half = jnp.dot(chol_vectors[0], coeff, preferred_element_type=jnp.float32).astype(
        jnp.bfloat16
    )

    pair_h = y_pair(half, nrow, ring)
    partner_h = lax.ppermute(pair_h, "aux", partner)
    quad = jnp.stack([pair_h, partner_h])
    stream_h = one_way_ring(quad, naux, nrow, ring)
    swapped_h = lax.ppermute(stream_h[:, 1], "aux", partner)
    all_h = jnp.concatenate([pair_h[None], stream_h[:, 0], swapped_h]).reshape(
        (-1, block, nocc)
    )

    chosen = tile_pairs[tile_owner[0]]
    left_rows = jnp.take(all_h, slot_of(chosen[:, 0], z, core, ring), axis=0)
    right_rows = jnp.take(all_h, slot_of(chosen[:, 1], z, core, ring), axis=0)
    partial_tiles = jnp.einsum(
        "sao,sbo->sab", left_rows, right_rows, preferred_element_type=jnp.float32
    )
    slots = partial_tiles.shape[0]
    split = partial_tiles.reshape(slots, naux, block // naux, block).transpose(1, 0, 2, 3)
    pieces = lax.all_to_all(split, "aux", 0, 0, tiled=True)
    return jnp.sum(pieces, axis=0)


def solution(mesh):
    placed = (P("aux", "row", None), P("row", None), P(), P("row", None))
    return jax.shard_map(
        local, mesh=mesh, in_specs=placed, out_specs=P("row", "aux", None), check_vma=False
    )
```

```python
import jax
import jax.numpy as jnp
from jax import lax
from jax.sharding import PartitionSpec as P


def ring_gather(x, nrow, ring):
    pairs = nrow // ring
    r = lax.axis_index("row")
    yh = r // ring
    z = r % ring
    other = lax.ppermute(x, "row", [(i, i ^ ring) for i in range(nrow)])
    pair = jnp.where(yh == 0, jnp.stack([x, other]), jnp.stack([other, x]))
    send_right = [(i, (i // ring) * ring + (i % ring + 1) % ring) for i in range(nrow)]
    send_left = [(i, (i // ring) * ring + (i % ring - 1) % ring) for i in range(nrow)]
    got = [None] * ring
    got[0] = pair
    from_left = pair
    from_right = pair
    for t in range(1, ring // 2):
        from_left = lax.ppermute(from_left, "row", send_right)
        from_right = lax.ppermute(from_right, "row", send_left)
        got[t] = from_left
        got[ring - t] = from_right
    low = lax.ppermute(from_left[0], "row", send_right)
    high = lax.ppermute(from_right[1], "row", send_left)
    got[ring // 2] = jnp.stack([low, high])
    stacked = jnp.stack(got)
    return stacked.reshape((ring * pairs,) + x.shape), z


def position_of(k, z, ring):
    return ((z - k % ring) % ring) * 2 + k // ring


def reduce_scatter_aux(parts, naux):
    nx = naux // 4
    me = lax.axis_index("aux")
    c_me = me % 2
    y_me = (me // 2) % 2
    x_me = me // 4
    shaped = parts.reshape((parts.shape[0], nx, 2, 2) + parts.shape[2:])
    keep = jnp.take(shaped, c_me, axis=3)
    send = jnp.take(shaped, 1 - c_me, axis=3)
    on_chip = keep + lax.ppermute(send, "aux", [(i, i ^ 1) for i in range(naux)])
    total = jnp.take(on_chip, x_me, axis=1)
    for dx in range(1, nx):
        perm = [(i, ((i // 4 + dx) % nx) * 4 + i % 4) for i in range(naux)]
        total = total + lax.ppermute(
            jnp.take(on_chip, (x_me + dx) % nx, axis=1), "aux", perm
        )
    mine = jnp.take(total, y_me, axis=1)
    theirs = jnp.take(total, 1 - y_me, axis=1)
    return mine + lax.ppermute(theirs, "aux", [(i, i ^ 2) for i in range(naux)])


def local(chol_vectors, occ_coeff, tile_pairs, tile_owner):
    block = chol_vectors.shape[1]
    nbf = chol_vectors.shape[2]
    nocc = occ_coeff.shape[1]
    nrow = lax.axis_size("row")
    naux = lax.axis_size("aux")
    ring = nrow // 2
    half_cols = nocc // 2

    core = lax.axis_index("aux") % 2
    mine = lax.dynamic_slice_in_dim(occ_coeff, core * half_cols, half_cols, 1)
    mine_ring, z = ring_gather(mine, nrow, ring)
    partner = [(i, i ^ 1) for i in range(naux)]
    other_ring = lax.ppermute(mine_ring, "aux", partner)
    coeff_ring = jnp.where(
        core == 0,
        jnp.concatenate([mine_ring, other_ring], axis=2),
        jnp.concatenate([other_ring, mine_ring], axis=2),
    )

    p = jnp.arange(nrow)
    block_at = (p % 2) * ring + (z - p // 2) % ring
    chol = chol_vectors[0].reshape(block, nrow, nbf // nrow)
    chol_ring = jnp.take(chol, block_at, axis=1).reshape(block, nbf)
    half = jnp.dot(
        chol_ring, coeff_ring.reshape(nbf, nocc), preferred_element_type=jnp.float32
    ).astype(jnp.bfloat16)

    half_ring, _ = ring_gather(half, nrow, ring)
    chosen = tile_pairs[tile_owner[0]]
    left_rows = jnp.take(half_ring, position_of(chosen[:, 0], z, ring), axis=0)
    right_rows = jnp.take(half_ring, position_of(chosen[:, 1], z, ring), axis=0)
    partial_tiles = jnp.einsum(
        "sao,sbo->sab", left_rows, right_rows, preferred_element_type=jnp.float32
    )
    slots = partial_tiles.shape[0]
    split = partial_tiles.reshape(slots, naux, block // naux, block)
    return reduce_scatter_aux(split, naux)


def solution(mesh):
    placed = (P("aux", "row", None), P("row", None), P(), P("row", None))
    return jax.shard_map(
        local, mesh=mesh, in_specs=placed, out_specs=P("row", "aux", None), check_vma=False
    )
```

```python
import jax
import jax.numpy as jnp
from jax import lax
from jax.sharding import PartitionSpec as P


def ring_gather(x, nrow, ring):
    r = lax.axis_index("row")
    z = r % ring
    send_right = [(i, (i // ring) * ring + (i % ring + 1) % ring) for i in range(nrow)]
    send_left = [(i, (i // ring) * ring + (i % ring - 1) % ring) for i in range(nrow)]
    across = [(i, i ^ ring) for i in range(nrow)]
    own = [None] * ring
    far = [None] * ring
    own[0] = x
    far[0] = lax.ppermute(x, "row", across)
    from_left = lax.ppermute(x, "row", send_right)
    from_right = lax.ppermute(x, "row", send_left)
    own[1] = from_left
    own[ring - 1] = from_right
    for t in range(2, ring // 2):
        far[t - 1] = lax.ppermute(from_left, "row", across)
        far[ring - t + 1] = lax.ppermute(from_right, "row", across)
        from_left = lax.ppermute(from_left, "row", send_right)
        from_right = lax.ppermute(from_right, "row", send_left)
        own[t] = from_left
        own[ring - t] = from_right
    t = ring // 2
    far[t - 1] = lax.ppermute(from_left, "row", across)
    far[ring - t + 1] = lax.ppermute(from_right, "row", across)
    own[t] = lax.ppermute(from_left, "row", send_right)
    far[t] = lax.ppermute(own[t], "row", across)
    return jnp.stack(own + far), z


def position_of(k, z, ring):
    yh = lax.axis_index("row") // ring
    return jnp.where(k // ring == yh, 0, ring) + (z - k % ring) % ring


def reduce_scatter_aux(parts, naux):
    nx = naux // 4
    me = lax.axis_index("aux")
    c_me = me % 2
    y_me = (me // 2) % 2
    x_me = me // 4
    shaped = parts.reshape((parts.shape[0], nx, 2, 2) + parts.shape[2:])
    keep = jnp.take(shaped, c_me, axis=3)
    send = jnp.take(shaped, 1 - c_me, axis=3)
    on_chip = keep + lax.ppermute(send, "aux", [(i, i ^ 1) for i in range(naux)])
    total = jnp.take(on_chip, x_me, axis=1)
    for dx in range(1, nx):
        perm = [(i, ((i // 4 + dx) % nx) * 4 + i % 4) for i in range(naux)]
        total = total + lax.ppermute(
            jnp.take(on_chip, (x_me + dx) % nx, axis=1), "aux", perm
        )
    mine = jnp.take(total, y_me, axis=1)
    theirs = jnp.take(total, 1 - y_me, axis=1)
    return mine + lax.ppermute(theirs, "aux", [(i, i ^ 2) for i in range(naux)])


def local(chol_vectors, occ_coeff, tile_pairs, tile_owner):
    block = chol_vectors.shape[1]
    nbf = chol_vectors.shape[2]
    nocc = occ_coeff.shape[1]
    nrow = lax.axis_size("row")
    naux = lax.axis_size("aux")
    ring = nrow // 2
    half_cols = nocc // 2

    core = lax.axis_index("aux") % 2
    mine = lax.dynamic_slice_in_dim(occ_coeff, core * half_cols, half_cols, 1)
    mine_ring, z = ring_gather(mine, nrow, ring)
    partner = [(i, i ^ 1) for i in range(naux)]
    other_ring = lax.ppermute(mine_ring, "aux", partner)

    p = jnp.arange(nrow)
    yh = lax.axis_index("row") // ring
    block_at = jnp.where(p // ring == 0, yh, 1 - yh) * ring + (z - p % ring) % ring
    chol = chol_vectors[0].reshape(block, nrow, nbf // nrow)
    chol_ring = jnp.take(chol, block_at, axis=1).reshape(block, nbf)
    half_mine = jnp.dot(
        chol_ring, mine_ring.reshape(nbf, half_cols), preferred_element_type=jnp.float32
    )
    half_other = jnp.dot(
        chol_ring, other_ring.reshape(nbf, half_cols), preferred_element_type=jnp.float32
    )
    half = jnp.where(
        core == 0,
        jnp.concatenate([half_mine, half_other], axis=1),
        jnp.concatenate([half_other, half_mine], axis=1),
    ).astype(jnp.bfloat16)

    half_ring, _ = ring_gather(half, nrow, ring)
    chosen = tile_pairs[tile_owner[0]]
    left_rows = jnp.take(half_ring, position_of(chosen[:, 0], z, ring), axis=0)
    right_rows = jnp.take(half_ring, position_of(chosen[:, 1], z, ring), axis=0)
    partial_tiles = jnp.einsum(
        "sao,sbo->sab", left_rows, right_rows, preferred_element_type=jnp.float32
    )
    slots = partial_tiles.shape[0]
    split = partial_tiles.reshape(slots, naux, block // naux, block)
    return reduce_scatter_aux(split, naux)


def solution(mesh):
    placed = (P("aux", "row", None), P("row", None), P(), P("row", None))
    return jax.shard_map(
        local, mesh=mesh, in_specs=placed, out_specs=P("row", "aux", None), check_vma=False
    )
```

```python
import jax
import jax.numpy as jnp
from jax import lax
from jax.sharding import PartitionSpec as P


def ring_gather(x, nrow, ring):
    pairs = nrow // ring
    r = lax.axis_index("row")
    yh = r // ring
    z = r % ring
    other = lax.ppermute(x, "row", [(i, i ^ ring) for i in range(nrow)])
    pair = jnp.where(yh == 0, jnp.stack([x, other]), jnp.stack([other, x]))
    send_right = [(i, (i // ring) * ring + (i % ring + 1) % ring) for i in range(nrow)]
    send_left = [(i, (i // ring) * ring + (i % ring - 1) % ring) for i in range(nrow)]
    got = [None] * ring
    got[0] = pair
    from_left = pair
    from_right = pair
    for t in range(1, ring // 2):
        from_left = lax.ppermute(from_left, "row", send_right)
        from_right = lax.ppermute(from_right, "row", send_left)
        got[t] = from_left
        got[ring - t] = from_right
    low = lax.ppermute(from_left[0], "row", send_right)
    high = lax.ppermute(from_right[1], "row", send_left)
    got[ring // 2] = jnp.stack([low, high])
    stacked = jnp.stack(got)
    return stacked.reshape((ring * pairs,) + x.shape), z


def position_of(k, z, ring):
    return ((z - k % ring) % ring) * 2 + k // ring


def reduce_scatter_aux(parts, naux):
    nx = naux // 4
    slots, rows, cols = parts.shape
    me = lax.axis_index("aux")
    c_me = me % 2
    y_me = (me // 2) % 2
    x_me = me // 4
    shaped = parts.reshape(slots, 2, rows // 2, cols)
    keep = jnp.take(shaped, c_me, axis=1)
    send = jnp.take(shaped, 1 - c_me, axis=1)
    on_chip = keep + lax.ppermute(send, "aux", [(i, i ^ 1) for i in range(naux)])
    on_chip = on_chip.reshape(slots, nx, rows // (2 * nx), cols)
    total = jnp.take(on_chip, x_me, axis=1)
    for dx in range(1, nx):
        perm = [(i, ((i // 4 + dx) % nx) * 4 + i % 4) for i in range(naux)]
        total = total + lax.ppermute(
            jnp.take(on_chip, (x_me + dx) % nx, axis=1), "aux", perm
        )
    total = total.reshape(slots, 2, rows // naux, cols)
    mine = jnp.take(total, y_me, axis=1)
    theirs = jnp.take(total, 1 - y_me, axis=1)
    return mine + lax.ppermute(theirs, "aux", [(i, i ^ 2) for i in range(naux)])


def local(chol_vectors, occ_coeff, tile_pairs, tile_owner):
    block = chol_vectors.shape[1]
    nbf = chol_vectors.shape[2]
    nocc = occ_coeff.shape[1]
    nrow = lax.axis_size("row")
    naux = lax.axis_size("aux")
    ring = nrow // 2
    half_cols = nocc // 2

    core = lax.axis_index("aux") % 2
    mine = lax.dynamic_slice_in_dim(occ_coeff, core * half_cols, half_cols, 1)
    mine_ring, z = ring_gather(mine, nrow, ring)
    partner = [(i, i ^ 1) for i in range(naux)]
    other_ring = lax.ppermute(mine_ring, "aux", partner)

    p = jnp.arange(nrow)
    block_at = (p % 2) * ring + (z - p // 2) % ring
    chol = chol_vectors[0].reshape(block, nrow, nbf // nrow)
    chol_ring = jnp.take(chol, block_at, axis=1).reshape(block, nbf)
    half_mine = jnp.dot(
        chol_ring, mine_ring.reshape(nbf, half_cols), preferred_element_type=jnp.float32
    )
    half_other = jnp.dot(
        chol_ring, other_ring.reshape(nbf, half_cols), preferred_element_type=jnp.float32
    )
    half = jnp.where(
        core == 0,
        jnp.concatenate([half_mine, half_other], axis=1),
        jnp.concatenate([half_other, half_mine], axis=1),
    ).astype(jnp.bfloat16)

    half_ring, _ = ring_gather(half, nrow, ring)
    chosen = tile_pairs[tile_owner[0]]
    left_rows = jnp.take(half_ring, position_of(chosen[:, 0], z, ring), axis=0)
    slots = left_rows.shape[0]
    left_rows = (
        left_rows.reshape(slots, naux // 4, 2, 2, block // naux, nocc)
        .transpose(0, 3, 1, 2, 4, 5)
        .reshape(slots, block, nocc)
    )
    right_rows = jnp.take(half_ring, position_of(chosen[:, 1], z, ring), axis=0)
    partial_tiles = jnp.einsum(
        "sao,sbo->sab", left_rows, right_rows, preferred_element_type=jnp.float32
    )
    return reduce_scatter_aux(partial_tiles, naux)


def solution(mesh):
    placed = (P("aux", "row", None), P("row", None), P(), P("row", None))
    return jax.shard_map(
        local, mesh=mesh, in_specs=placed, out_specs=P("row", "aux", None), check_vma=False
    )
```

```python
import jax
import jax.numpy as jnp
from jax import lax
from jax.sharding import PartitionSpec as P


def ring_gather(x, nrow, ring):
    pairs = nrow // ring
    r = lax.axis_index("row")
    yh = r // ring
    z = r % ring
    other = lax.ppermute(x, "row", [(i, i ^ ring) for i in range(nrow)])
    pair = jnp.where(yh == 0, jnp.stack([x, other]), jnp.stack([other, x]))

    def shift(d):
        return [(i, (i // ring) * ring + (i % ring + d) % ring) for i in range(nrow)]

    steps = ring // 4
    got = [None] * ring
    got[0] = pair
    near_r = near_l = far_r = far_l = pair
    for t in range(1, steps + 1):
        hop = steps + 1 if t == 1 else 1
        near_r = lax.ppermute(near_r, "row", shift(1))
        near_l = lax.ppermute(near_l, "row", shift(-1))
        far_r = lax.ppermute(far_r, "row", shift(hop))
        got[t] = near_r
        got[ring - t] = near_l
        got[steps + t] = far_r
        if t < steps:
            far_l = lax.ppermute(far_l, "row", shift(-hop))
            got[ring - steps - t] = far_l
    stacked = jnp.stack(got)
    return stacked.reshape((ring * pairs,) + x.shape), z


def position_of(k, z, ring):
    return ((z - k % ring) % ring) * 2 + k // ring


def reduce_scatter_aux(parts, naux):
    nx = naux // 4
    me = lax.axis_index("aux")
    c_me = me % 2
    y_me = (me // 2) % 2
    x_me = me // 4
    shaped = parts.reshape((parts.shape[0], nx, 2, 2) + parts.shape[2:])
    keep = jnp.take(shaped, c_me, axis=3)
    send = jnp.take(shaped, 1 - c_me, axis=3)
    on_chip = keep + lax.ppermute(send, "aux", [(i, i ^ 1) for i in range(naux)])
    total = jnp.take(on_chip, x_me, axis=1)
    for dx in range(1, nx):
        perm = [(i, ((i // 4 + dx) % nx) * 4 + i % 4) for i in range(naux)]
        total = total + lax.ppermute(
            jnp.take(on_chip, (x_me + dx) % nx, axis=1), "aux", perm
        )
    mine = jnp.take(total, y_me, axis=1)
    theirs = jnp.take(total, 1 - y_me, axis=1)
    return mine + lax.ppermute(theirs, "aux", [(i, i ^ 2) for i in range(naux)])


def local(chol_vectors, occ_coeff, tile_pairs, tile_owner):
    block = chol_vectors.shape[1]
    nbf = chol_vectors.shape[2]
    nocc = occ_coeff.shape[1]
    nrow = lax.axis_size("row")
    naux = lax.axis_size("aux")
    ring = nrow // 2
    half_cols = nocc // 2

    core = lax.axis_index("aux") % 2
    mine = lax.dynamic_slice_in_dim(occ_coeff, core * half_cols, half_cols, 1)
    mine_ring, z = ring_gather(mine, nrow, ring)
    partner = [(i, i ^ 1) for i in range(naux)]
    other_ring = lax.ppermute(mine_ring, "aux", partner)
    coeff_ring = jnp.where(
        core == 0,
        jnp.concatenate([mine_ring, other_ring], axis=2),
        jnp.concatenate([other_ring, mine_ring], axis=2),
    )

    p = jnp.arange(nrow)
    block_at = (p % 2) * ring + (z - p // 2) % ring
    chol = chol_vectors[0].reshape(block, nrow, nbf // nrow)
    chol_ring = jnp.take(chol, block_at, axis=1).reshape(block, nbf)
    half = jnp.dot(
        chol_ring, coeff_ring.reshape(nbf, nocc), preferred_element_type=jnp.float32
    ).astype(jnp.bfloat16)

    half_ring, _ = ring_gather(half, nrow, ring)
    chosen = tile_pairs[tile_owner[0]]
    left_rows = jnp.take(half_ring, position_of(chosen[:, 0], z, ring), axis=0)
    right_rows = jnp.take(half_ring, position_of(chosen[:, 1], z, ring), axis=0)
    partial_tiles = jnp.einsum(
        "sao,sbo->sab", left_rows, right_rows, preferred_element_type=jnp.float32
    )
    slots = partial_tiles.shape[0]
    split = partial_tiles.reshape(slots, naux, block // naux, block)
    return reduce_scatter_aux(split, naux)


def solution(mesh):
    placed = (P("aux", "row", None), P("row", None), P(), P("row", None))
    return jax.shard_map(
        local, mesh=mesh, in_specs=placed, out_specs=P("row", "aux", None), check_vma=False
    )
```

```python
import jax
import jax.numpy as jnp
from jax import lax
from jax.sharding import PartitionSpec as P


def ring_gather(x, nrow, ring):
    pairs = nrow // ring
    r = lax.axis_index("row")
    yh = r // ring
    z = r % ring
    other = lax.ppermute(x, "row", [(i, i ^ ring) for i in range(nrow)])
    pair = jnp.where(yh == 0, jnp.stack([x, other]), jnp.stack([other, x]))
    send_right = [(i, (i // ring) * ring + (i % ring + 1) % ring) for i in range(nrow)]
    send_left = [(i, (i // ring) * ring + (i % ring - 1) % ring) for i in range(nrow)]
    got = [None] * ring
    got[0] = pair
    from_left = pair
    from_right = pair
    for t in range(1, ring // 2):
        from_left = lax.ppermute(from_left, "row", send_right)
        from_right = lax.ppermute(from_right, "row", send_left)
        got[t] = from_left
        got[ring - t] = from_right
    low = lax.ppermute(from_left[0], "row", send_right)
    high = lax.ppermute(from_right[1], "row", send_left)
    got[ring // 2] = jnp.stack([low, high])
    stacked = jnp.stack(got)
    return stacked.reshape((ring * pairs,) + x.shape), z


def ring_gather_jump(x, nrow, ring):
    pairs = nrow // ring
    r = lax.axis_index("row")
    yh = r // ring
    z = r % ring
    other = lax.ppermute(x, "row", [(i, i ^ ring) for i in range(nrow)])
    pair = jnp.where(yh == 0, jnp.stack([x, other]), jnp.stack([other, x]))

    def shift(d):
        return [(i, (i // ring) * ring + (i % ring + d) % ring) for i in range(nrow)]

    steps = ring // 4
    got = [None] * ring
    got[0] = pair
    near_r = near_l = far_r = far_l = pair
    for t in range(1, steps + 1):
        hop = steps + 1 if t == 1 else 1
        near_r = lax.ppermute(near_r, "row", shift(1))
        near_l = lax.ppermute(near_l, "row", shift(-1))
        far_r = lax.ppermute(far_r, "row", shift(hop))
        got[t] = near_r
        got[ring - t] = near_l
        got[steps + t] = far_r
        if t < steps:
            far_l = lax.ppermute(far_l, "row", shift(-hop))
            got[ring - steps - t] = far_l
    stacked = jnp.stack(got)
    return stacked.reshape((ring * pairs,) + x.shape), z


def position_of(k, z, ring):
    return ((z - k % ring) % ring) * 2 + k // ring


def reduce_scatter_aux(parts, naux):
    nx = naux // 4
    me = lax.axis_index("aux")
    c_me = me % 2
    y_me = (me // 2) % 2
    x_me = me // 4
    shaped = parts.reshape((parts.shape[0], nx, 2, 2) + parts.shape[2:])
    keep = jnp.take(shaped, c_me, axis=3)
    send = jnp.take(shaped, 1 - c_me, axis=3)
    on_chip = keep + lax.ppermute(send, "aux", [(i, i ^ 1) for i in range(naux)])
    total = jnp.take(on_chip, x_me, axis=1)
    for dx in range(1, nx):
        perm = [(i, ((i // 4 + dx) % nx) * 4 + i % 4) for i in range(naux)]
        total = total + lax.ppermute(
            jnp.take(on_chip, (x_me + dx) % nx, axis=1), "aux", perm
        )
    mine = jnp.take(total, y_me, axis=1)
    theirs = jnp.take(total, 1 - y_me, axis=1)
    return mine + lax.ppermute(theirs, "aux", [(i, i ^ 2) for i in range(naux)])


def local(chol_vectors, occ_coeff, tile_pairs, tile_owner):
    block = chol_vectors.shape[1]
    nbf = chol_vectors.shape[2]
    nocc = occ_coeff.shape[1]
    nrow = lax.axis_size("row")
    naux = lax.axis_size("aux")
    ring = nrow // 2
    half_cols = nocc // 2

    core = lax.axis_index("aux") % 2
    mine = lax.dynamic_slice_in_dim(occ_coeff, core * half_cols, half_cols, 1)
    mine_ring, z = ring_gather_jump(mine, nrow, ring)
    partner = [(i, i ^ 1) for i in range(naux)]
    other_ring = lax.ppermute(mine_ring, "aux", partner)
    coeff_ring = jnp.where(
        core == 0,
        jnp.concatenate([mine_ring, other_ring], axis=2),
        jnp.concatenate([other_ring, mine_ring], axis=2),
    )

    p = jnp.arange(nrow)
    block_at = (p % 2) * ring + (z - p // 2) % ring
    chol = chol_vectors[0].reshape(block, nrow, nbf // nrow)
    chol_ring = jnp.take(chol, block_at, axis=1).reshape(block, nbf)
    half = jnp.dot(
        chol_ring, coeff_ring.reshape(nbf, nocc), preferred_element_type=jnp.float32
    ).astype(jnp.bfloat16)

    half_ring, _ = ring_gather(half, nrow, ring)
    chosen = tile_pairs[tile_owner[0]]
    left_rows = jnp.take(half_ring, position_of(chosen[:, 0], z, ring), axis=0)
    right_rows = jnp.take(half_ring, position_of(chosen[:, 1], z, ring), axis=0)
    partial_tiles = jnp.einsum(
        "sao,sbo->sab", left_rows, right_rows, preferred_element_type=jnp.float32
    )
    slots = partial_tiles.shape[0]
    split = partial_tiles.reshape(slots, naux, block // naux, block)
    return reduce_scatter_aux(split, naux)


def solution(mesh):
    placed = (P("aux", "row", None), P("row", None), P(), P("row", None))
    return jax.shard_map(
        local, mesh=mesh, in_specs=placed, out_specs=P("row", "aux", None), check_vma=False
    )
```

```python
import jax
import jax.numpy as jnp
from jax import lax
from jax.sharding import PartitionSpec as P


def ring_gather(x, nrow, ring):
    pairs = nrow // ring
    r = lax.axis_index("row")
    yh = r // ring
    z = r % ring
    other = lax.ppermute(x, "row", [(i, i ^ ring) for i in range(nrow)])
    pair = jnp.where(yh == 0, jnp.stack([x, other]), jnp.stack([other, x]))
    send_right = [(i, (i // ring) * ring + (i % ring + 1) % ring) for i in range(nrow)]
    send_left = [(i, (i // ring) * ring + (i % ring - 1) % ring) for i in range(nrow)]
    got = [None] * ring
    got[0] = pair
    from_left = pair
    from_right = pair
    for t in range(1, ring // 2):
        from_left = lax.ppermute(from_left, "row", send_right)
        from_right = lax.ppermute(from_right, "row", send_left)
        got[t] = from_left
        got[ring - t] = from_right
    low = lax.ppermute(from_left[0], "row", send_right)
    high = lax.ppermute(from_right[1], "row", send_left)
    got[ring // 2] = jnp.stack([low, high])
    stacked = jnp.stack(got)
    return stacked.reshape((ring * pairs,) + x.shape), z


def ring_gather_jump(x, nrow, ring):
    pairs = nrow // ring
    r = lax.axis_index("row")
    yh = r // ring
    z = r % ring
    other = lax.ppermute(x, "row", [(i, i ^ ring) for i in range(nrow)])
    pair = jnp.where(yh == 0, jnp.stack([x, other]), jnp.stack([other, x]))

    def shift(d):
        return [(i, (i // ring) * ring + (i % ring + d) % ring) for i in range(nrow)]

    steps = ring // 4
    got = [None] * ring
    got[0] = pair
    near_r = near_l = far_r = far_l = pair
    for t in range(1, steps + 1):
        hop = steps + 1 if t == 1 else 1
        near_r = lax.ppermute(near_r, "row", shift(1))
        near_l = lax.ppermute(near_l, "row", shift(-1))
        far_r = lax.ppermute(far_r, "row", shift(hop))
        got[t] = near_r
        got[ring - t] = near_l
        got[steps + t] = far_r
        if t < steps:
            far_l = lax.ppermute(far_l, "row", shift(-hop))
            got[ring - steps - t] = far_l
    stacked = jnp.stack(got)
    return stacked.reshape((ring * pairs,) + x.shape), z


def position_of(k, z, ring):
    return ((z - k % ring) % ring) * 2 + k // ring


def reduce_scatter_aux(parts, naux):
    nx = naux // 4
    slots, rows, cols = parts.shape
    per = rows // naux
    me = lax.axis_index("aux")
    c_me = me % 2
    y_me = (me // 2) % 2
    x_me = me // 4
    shaped = parts.reshape(slots, nx * 2, 2 * per, cols)
    keep = lax.dynamic_slice_in_dim(shaped, c_me * per, per, axis=2)
    send = lax.dynamic_slice_in_dim(shaped, (1 - c_me) * per, per, axis=2)
    on_chip = keep + lax.ppermute(send, "aux", [(i, i ^ 1) for i in range(naux)])
    on_chip = on_chip.reshape(slots, nx, 2, per, cols)
    total = jnp.take(on_chip, x_me, axis=1)
    for dx in range(1, nx):
        perm = [(i, ((i // 4 + dx) % nx) * 4 + i % 4) for i in range(naux)]
        total = total + lax.ppermute(
            jnp.take(on_chip, (x_me + dx) % nx, axis=1), "aux", perm
        )
    mine = jnp.take(total, y_me, axis=1)
    theirs = jnp.take(total, 1 - y_me, axis=1)
    return mine + lax.ppermute(theirs, "aux", [(i, i ^ 2) for i in range(naux)])


def local(chol_vectors, occ_coeff, tile_pairs, tile_owner):
    block = chol_vectors.shape[1]
    nbf = chol_vectors.shape[2]
    nocc = occ_coeff.shape[1]
    nrow = lax.axis_size("row")
    naux = lax.axis_size("aux")
    ring = nrow // 2
    half_cols = nocc // 2

    core = lax.axis_index("aux") % 2
    mine = lax.dynamic_slice_in_dim(occ_coeff, core * half_cols, half_cols, 1)
    mine_ring, z = ring_gather_jump(mine, nrow, ring)
    partner = [(i, i ^ 1) for i in range(naux)]
    other_ring = lax.ppermute(mine_ring, "aux", partner)
    coeff_ring = jnp.where(
        core == 0,
        jnp.concatenate([mine_ring, other_ring], axis=2),
        jnp.concatenate([other_ring, mine_ring], axis=2),
    )

    p = jnp.arange(nrow)
    block_at = (p % 2) * ring + (z - p // 2) % ring
    chol = chol_vectors[0].reshape(block, nrow, nbf // nrow)
    chol_ring = jnp.take(chol, block_at, axis=1).reshape(block, nbf)
    half = jnp.dot(
        chol_ring, coeff_ring.reshape(nbf, nocc), preferred_element_type=jnp.float32
    ).astype(jnp.bfloat16)

    half_ring, _ = ring_gather(half, nrow, ring)
    chosen = tile_pairs[tile_owner[0]]
    left_rows = jnp.take(half_ring, position_of(chosen[:, 0], z, ring), axis=0)
    right_rows = jnp.take(half_ring, position_of(chosen[:, 1], z, ring), axis=0)
    partial_tiles = jnp.einsum(
        "sao,sbo->sab", left_rows, right_rows, preferred_element_type=jnp.float32
    )
    return reduce_scatter_aux(partial_tiles, naux)


def solution(mesh):
    placed = (P("aux", "row", None), P("row", None), P(), P("row", None))
    return jax.shard_map(
        local, mesh=mesh, in_specs=placed, out_specs=P("row", "aux", None), check_vma=False
    )
```

```python
import jax
import jax.numpy as jnp
from jax import lax
from jax.sharding import PartitionSpec as P


def ring_gather(x, nrow, ring):
    pairs = nrow // ring
    r = lax.axis_index("row")
    yh = r // ring
    z = r % ring
    other = lax.ppermute(x, "row", [(i, i ^ ring) for i in range(nrow)])
    pair = jnp.where(yh == 0, jnp.stack([x, other]), jnp.stack([other, x]))
    send_right = [(i, (i // ring) * ring + (i % ring + 1) % ring) for i in range(nrow)]
    send_left = [(i, (i // ring) * ring + (i % ring - 1) % ring) for i in range(nrow)]
    got = [None] * ring
    got[0] = pair
    from_left = pair
    from_right = pair
    for t in range(1, ring // 2):
        from_left = lax.ppermute(from_left, "row", send_right)
        from_right = lax.ppermute(from_right, "row", send_left)
        got[t] = from_left
        got[ring - t] = from_right
    low = lax.ppermute(from_left[0], "row", send_right)
    high = lax.ppermute(from_right[1], "row", send_left)
    got[ring // 2] = jnp.stack([low, high])
    stacked = jnp.stack(got)
    return stacked.reshape((ring * pairs,) + x.shape), z


def ring_gather_jump(x, nrow, ring):
    pairs = nrow // ring
    r = lax.axis_index("row")
    yh = r // ring
    z = r % ring
    other = lax.ppermute(x, "row", [(i, i ^ ring) for i in range(nrow)])
    pair = jnp.where(yh == 0, jnp.stack([x, other]), jnp.stack([other, x]))

    def shift(d):
        return [(i, (i // ring) * ring + (i % ring + d) % ring) for i in range(nrow)]

    steps = ring // 4
    got = [None] * ring
    got[0] = pair
    near_r = near_l = far_r = far_l = pair
    for t in range(1, steps + 1):
        hop = steps + 1 if t == 1 else 1
        near_r = lax.ppermute(near_r, "row", shift(1))
        near_l = lax.ppermute(near_l, "row", shift(-1))
        far_r = lax.ppermute(far_r, "row", shift(hop))
        got[t] = near_r
        got[ring - t] = near_l
        got[steps + t] = far_r
        if t < steps:
            far_l = lax.ppermute(far_l, "row", shift(-hop))
            got[ring - steps - t] = far_l
    stacked = jnp.stack(got)
    return stacked.reshape((ring * pairs,) + x.shape), z


def position_of(k, z, ring):
    return ((z - k % ring) % ring) * 2 + k // ring


def reduce_scatter_aux(parts, naux):
    nx = naux // 4
    slots, rows, cols = parts.shape
    per = rows // naux
    me = lax.axis_index("aux")
    c_me = me % 2
    y_me = (me // 2) % 2
    x_me = me // 4
    shaped = parts.reshape(slots, nx * 2, 2 * per, cols)
    keep = lax.dynamic_slice_in_dim(shaped, c_me * per, per, axis=2)
    send = lax.dynamic_slice_in_dim(shaped, (1 - c_me) * per, per, axis=2)
    on_chip = keep + lax.ppermute(send, "aux", [(i, i ^ 1) for i in range(naux)])
    total = lax.dynamic_slice_in_dim(on_chip, x_me * 2, 2, axis=1)
    for dx in range(1, nx):
        perm = [(i, ((i // 4 + dx) % nx) * 4 + i % 4) for i in range(naux)]
        total = total + lax.ppermute(
            lax.dynamic_slice_in_dim(on_chip, ((x_me + dx) % nx) * 2, 2, axis=1),
            "aux",
            perm,
        )
    mine = jnp.take(total, y_me, axis=1)
    theirs = jnp.take(total, 1 - y_me, axis=1)
    return mine + lax.ppermute(theirs, "aux", [(i, i ^ 2) for i in range(naux)])


def local(chol_vectors, occ_coeff, tile_pairs, tile_owner):
    block = chol_vectors.shape[1]
    nbf = chol_vectors.shape[2]
    nocc = occ_coeff.shape[1]
    nrow = lax.axis_size("row")
    naux = lax.axis_size("aux")
    ring = nrow // 2
    half_cols = nocc // 2

    core = lax.axis_index("aux") % 2
    mine = lax.dynamic_slice_in_dim(occ_coeff, core * half_cols, half_cols, 1)
    mine_ring, z = ring_gather_jump(mine, nrow, ring)
    partner = [(i, i ^ 1) for i in range(naux)]
    other_ring = lax.ppermute(mine_ring, "aux", partner)
    coeff_ring = jnp.where(
        core == 0,
        jnp.concatenate([mine_ring, other_ring], axis=2),
        jnp.concatenate([other_ring, mine_ring], axis=2),
    )

    p = jnp.arange(nrow)
    block_at = (p % 2) * ring + (z - p // 2) % ring
    chol = chol_vectors[0].reshape(block, nrow, nbf // nrow)
    chol_ring = jnp.take(chol, block_at, axis=1).reshape(block, nbf)
    half = jnp.dot(
        chol_ring, coeff_ring.reshape(nbf, nocc), preferred_element_type=jnp.float32
    ).astype(jnp.bfloat16)

    half_ring, _ = ring_gather(half, nrow, ring)
    chosen = tile_pairs[tile_owner[0]]
    left_rows = jnp.take(half_ring, position_of(chosen[:, 0], z, ring), axis=0)
    right_rows = jnp.take(half_ring, position_of(chosen[:, 1], z, ring), axis=0)
    partial_tiles = jnp.einsum(
        "sao,sbo->sab", left_rows, right_rows, preferred_element_type=jnp.float32
    )
    return reduce_scatter_aux(partial_tiles, naux)


def solution(mesh):
    placed = (P("aux", "row", None), P("row", None), P(), P("row", None))
    return jax.shard_map(
        local, mesh=mesh, in_specs=placed, out_specs=P("row", "aux", None), check_vma=False
    )
```

```python
import jax
import jax.numpy as jnp
from jax import lax
from jax.sharding import PartitionSpec as P


def ring_gather(x, nrow, ring):
    pairs = nrow // ring
    r = lax.axis_index("row")
    yh = r // ring
    z = r % ring
    other = lax.ppermute(x, "row", [(i, i ^ ring) for i in range(nrow)])
    pair = jnp.where(yh == 0, jnp.stack([x, other]), jnp.stack([other, x]))
    send_right = [(i, (i // ring) * ring + (i % ring + 1) % ring) for i in range(nrow)]
    send_left = [(i, (i // ring) * ring + (i % ring - 1) % ring) for i in range(nrow)]
    got = [None] * ring
    got[0] = pair
    from_left = pair
    from_right = pair
    for t in range(1, ring // 2):
        from_left = lax.ppermute(from_left, "row", send_right)
        from_right = lax.ppermute(from_right, "row", send_left)
        got[t] = from_left
        got[ring - t] = from_right
    low = lax.ppermute(from_left[0], "row", send_right)
    high = lax.ppermute(from_right[1], "row", send_left)
    got[ring // 2] = jnp.stack([low, high])
    stacked = jnp.stack(got)
    return stacked.reshape((ring * pairs,) + x.shape), z


def ring_gather_jump(x, nrow, ring):
    pairs = nrow // ring
    r = lax.axis_index("row")
    yh = r // ring
    z = r % ring
    other = lax.ppermute(x, "row", [(i, i ^ ring) for i in range(nrow)])
    pair = jnp.where(yh == 0, jnp.stack([x, other]), jnp.stack([other, x]))

    def shift(d):
        return [(i, (i // ring) * ring + (i % ring + d) % ring) for i in range(nrow)]

    steps = ring // 4
    got = [None] * ring
    got[0] = pair
    near_r = near_l = far_r = far_l = pair
    for t in range(1, steps + 1):
        hop = steps + 1 if t == 1 else 1
        near_r = lax.ppermute(near_r, "row", shift(1))
        near_l = lax.ppermute(near_l, "row", shift(-1))
        far_r = lax.ppermute(far_r, "row", shift(hop))
        got[t] = near_r
        got[ring - t] = near_l
        got[steps + t] = far_r
        if t < steps:
            far_l = lax.ppermute(far_l, "row", shift(-hop))
            got[ring - steps - t] = far_l
    stacked = jnp.stack(got)
    return stacked.reshape((ring * pairs,) + x.shape), z


def position_of(k, z, ring):
    return ((z - k % ring) % ring) * 2 + k // ring


def reduce_scatter_aux(parts, naux):
    nx = naux // 4
    slots, rows, cols = parts.shape
    per = rows // naux
    me = lax.axis_index("aux")
    c_me = me % 2
    y_me = (me // 2) % 2
    x_me = me // 4
    shaped = parts.reshape(slots, nx * 2, 2 * per, cols)
    keep = lax.dynamic_slice_in_dim(shaped, c_me * per, per, axis=2)
    send = lax.dynamic_slice_in_dim(shaped, (1 - c_me) * per, per, axis=2)
    on_chip = keep + lax.ppermute(send, "aux", [(i, i ^ 1) for i in range(naux)])
    total = lax.dynamic_slice_in_dim(on_chip, x_me * 2, 2, axis=1)
    for dx in sorted(range(1, nx), key=lambda d: -min(d, nx - d)):
        perm = [(i, ((i // 4 + dx) % nx) * 4 + i % 4) for i in range(naux)]
        total = total + lax.ppermute(
            lax.dynamic_slice_in_dim(on_chip, ((x_me + dx) % nx) * 2, 2, axis=1),
            "aux",
            perm,
        )
    mine = jnp.take(total, y_me, axis=1)
    theirs = jnp.take(total, 1 - y_me, axis=1)
    return mine + lax.ppermute(theirs, "aux", [(i, i ^ 2) for i in range(naux)])


def local(chol_vectors, occ_coeff, tile_pairs, tile_owner):
    block = chol_vectors.shape[1]
    nbf = chol_vectors.shape[2]
    nocc = occ_coeff.shape[1]
    nrow = lax.axis_size("row")
    naux = lax.axis_size("aux")
    ring = nrow // 2
    half_cols = nocc // 2

    core = lax.axis_index("aux") % 2
    mine = lax.dynamic_slice_in_dim(occ_coeff, core * half_cols, half_cols, 1)
    mine_ring, z = ring_gather_jump(mine, nrow, ring)
    partner = [(i, i ^ 1) for i in range(naux)]
    other_ring = lax.ppermute(mine_ring, "aux", partner)
    coeff_ring = jnp.where(
        core == 0,
        jnp.concatenate([mine_ring, other_ring], axis=2),
        jnp.concatenate([other_ring, mine_ring], axis=2),
    )

    p = jnp.arange(nrow)
    block_at = (p % 2) * ring + (z - p // 2) % ring
    chol = chol_vectors[0].reshape(block, nrow, nbf // nrow)
    chol_ring = jnp.take(chol, block_at, axis=1).reshape(block, nbf)
    half = jnp.dot(
        chol_ring, coeff_ring.reshape(nbf, nocc), preferred_element_type=jnp.float32
    ).astype(jnp.bfloat16)

    half_ring, _ = ring_gather(half, nrow, ring)
    chosen = tile_pairs[tile_owner[0]]
    left_rows = jnp.take(half_ring, position_of(chosen[:, 0], z, ring), axis=0)
    right_rows = jnp.take(half_ring, position_of(chosen[:, 1], z, ring), axis=0)
    partial_tiles = jnp.einsum(
        "sao,sbo->sab", left_rows, right_rows, preferred_element_type=jnp.float32
    )
    return reduce_scatter_aux(partial_tiles, naux)


def solution(mesh):
    placed = (P("aux", "row", None), P("row", None), P(), P("row", None))
    return jax.shard_map(
        local, mesh=mesh, in_specs=placed, out_specs=P("row", "aux", None), check_vma=False
    )
```

```python
import jax
import jax.numpy as jnp
from jax import lax
from jax.sharding import PartitionSpec as P


def ring_gather(x, nrow, ring):
    pairs = nrow // ring
    r = lax.axis_index("row")
    yh = r // ring
    z = r % ring
    other = lax.ppermute(x, "row", [(i, i ^ ring) for i in range(nrow)])
    pair = jnp.stack([x, other])
    send_right = [(i, (i // ring) * ring + (i % ring + 1) % ring) for i in range(nrow)]
    send_left = [(i, (i // ring) * ring + (i % ring - 1) % ring) for i in range(nrow)]
    got = [None] * ring
    got[0] = pair
    from_left = pair
    from_right = pair
    for t in range(1, ring // 2):
        from_left = lax.ppermute(from_left, "row", send_right)
        from_right = lax.ppermute(from_right, "row", send_left)
        got[t] = from_left
        got[ring - t] = from_right
    low = lax.ppermute(from_left[0], "row", send_right)
    high = lax.ppermute(from_right[1], "row", send_left)
    got[ring // 2] = jnp.stack([low, high])
    stacked = jnp.stack(got)
    return stacked.reshape((ring * pairs,) + x.shape), z


def ring_gather_jump(x, nrow, ring):
    pairs = nrow // ring
    r = lax.axis_index("row")
    yh = r // ring
    z = r % ring
    other = lax.ppermute(x, "row", [(i, i ^ ring) for i in range(nrow)])
    pair = jnp.stack([x, other])

    def shift(d):
        return [(i, (i // ring) * ring + (i % ring + d) % ring) for i in range(nrow)]

    steps = ring // 4
    got = [None] * ring
    got[0] = pair
    near_r = near_l = far_r = far_l = pair
    for t in range(1, steps + 1):
        hop = steps + 1 if t == 1 else 1
        near_r = lax.ppermute(near_r, "row", shift(1))
        near_l = lax.ppermute(near_l, "row", shift(-1))
        far_r = lax.ppermute(far_r, "row", shift(hop))
        got[t] = near_r
        got[ring - t] = near_l
        got[steps + t] = far_r
        if t < steps:
            far_l = lax.ppermute(far_l, "row", shift(-hop))
            got[ring - steps - t] = far_l
    stacked = jnp.stack(got)
    return stacked.reshape((ring * pairs,) + x.shape), z


def position_of(k, z, ring):
    yh = lax.axis_index("row") // ring
    return ((z - k % ring) % ring) * 2 + jnp.where(k // ring == yh, 0, 1)


def reduce_scatter_aux(parts, naux):
    nx = naux // 4
    slots, rows, cols = parts.shape
    per = rows // naux
    me = lax.axis_index("aux")
    c_me = me % 2
    y_me = (me // 2) % 2
    x_me = me // 4
    shaped = parts.reshape(slots, nx * 2, 2 * per, cols)
    keep = lax.dynamic_slice_in_dim(shaped, c_me * per, per, axis=2)
    send = lax.dynamic_slice_in_dim(shaped, (1 - c_me) * per, per, axis=2)
    on_chip = keep + lax.ppermute(send, "aux", [(i, i ^ 1) for i in range(naux)])
    total = lax.dynamic_slice_in_dim(on_chip, x_me * 2, 2, axis=1)
    for dx in sorted(range(1, nx), key=lambda d: -min(d, nx - d)):
        perm = [(i, ((i // 4 + dx) % nx) * 4 + i % 4) for i in range(naux)]
        total = total + lax.ppermute(
            lax.dynamic_slice_in_dim(on_chip, ((x_me + dx) % nx) * 2, 2, axis=1),
            "aux",
            perm,
        )
    mine = jnp.take(total, y_me, axis=1)
    theirs = jnp.take(total, 1 - y_me, axis=1)
    return mine + lax.ppermute(theirs, "aux", [(i, i ^ 2) for i in range(naux)])


def local(chol_vectors, occ_coeff, tile_pairs, tile_owner):
    block = chol_vectors.shape[1]
    nbf = chol_vectors.shape[2]
    nocc = occ_coeff.shape[1]
    nrow = lax.axis_size("row")
    naux = lax.axis_size("aux")
    ring = nrow // 2
    half_cols = nocc // 2

    core = lax.axis_index("aux") % 2
    mine = lax.dynamic_slice_in_dim(occ_coeff, core * half_cols, half_cols, 1)
    mine_ring, z = ring_gather_jump(mine, nrow, ring)
    partner = [(i, i ^ 1) for i in range(naux)]
    other_ring = lax.ppermute(mine_ring, "aux", partner)
    coeff_ring = jnp.where(
        core == 0,
        jnp.concatenate([mine_ring, other_ring], axis=2),
        jnp.concatenate([other_ring, mine_ring], axis=2),
    )

    p = jnp.arange(nrow)
    yh = lax.axis_index("row") // ring
    block_at = jnp.where(p % 2 == 0, yh, 1 - yh) * ring + (z - p // 2) % ring
    chol = chol_vectors[0].reshape(block, nrow, nbf // nrow)
    chol_ring = jnp.take(chol, block_at, axis=1).reshape(block, nbf)
    half = jnp.dot(
        chol_ring, coeff_ring.reshape(nbf, nocc), preferred_element_type=jnp.float32
    ).astype(jnp.bfloat16)

    half_ring, _ = ring_gather(half, nrow, ring)
    chosen = tile_pairs[tile_owner[0]]
    left_rows = jnp.take(half_ring, position_of(chosen[:, 0], z, ring), axis=0)
    right_rows = jnp.take(half_ring, position_of(chosen[:, 1], z, ring), axis=0)
    partial_tiles = jnp.einsum(
        "sao,sbo->sab", left_rows, right_rows, preferred_element_type=jnp.float32
    )
    return reduce_scatter_aux(partial_tiles, naux)


def solution(mesh):
    placed = (P("aux", "row", None), P("row", None), P(), P("row", None))
    return jax.shard_map(
        local, mesh=mesh, in_specs=placed, out_specs=P("row", "aux", None), check_vma=False
    )
```
